768 devices in a mesh: span: 8 (over y_lo, x), seq: 8 (over y_hi, core), mp: 12 (over z).
Axes of the slice: x: 4, y: 8 (y_hi: 4, y_lo: 2; y = y_hi * 2 + y_lo), z: 12, core: 2. Of those that a mesh axis runs over, the one named last changes fastest.
Arguments:
- queries: bfloat16 [8, 512, 6144], P('span', 'seq', 'mp'), may hold values from -30 to 30
- keys: bfloat16 [8, 512, 1024], P('span', 'seq'), may hold values from -30 to 30
- values: bfloat16 [8, 512, 1024], P('span', 'seq'), may hold values from -6 to 6
- clip_ids: int32 [512], P('seq'), may hold values from 0 to 5, never falling along the last dimension, each value on 1 to 256 neighbouring positions
- block_mask: int32 [8, 8], replicated, may hold values from 0 to 1, as said below
- out_weight: bfloat16 [6144, 6144], P('mp'), may hold values from -0.078125 to 0.078125
Outputs:
- projected: bfloat16 [8, 512, 6144], P('span', 'seq', 'mp')
The draws below stay inside these ranges and needn't reach their ends.
Inputs may be any that keep to these rules, and one draw needn't show every extreme that they name: block_mask[c][c] is 1; block_mask[c][c2] is 0 unless c - 3 < c2 <= c. `clip_ids`: clip ids never fall along the rows; each clip has 1 to 256 rows, one exactly that many.
All inputs are finite; a program needn't handle non-finite values.
Results may differ from the reference program's by a relative error of at most 0.017.
Values may be sent and summed in bfloat16 or wider, within the bound.
No kernel may reach another device: no remote copies, remote signals or barrier semaphores. Data moves between devices by JAX's collectives and lax.ppermute only.
A program may use at most 64 MiB of HBM per device.

```python
import math
import jax
import jax.numpy as jnp
import numpy as np
from jax import lax

D = 6144
HEADS = 48
HEAD_DIM = 128
WINDOW = 3
CLIPS = 6
GROUP = 6
KVD = 1024
NCHUNK = 8
ROWS = 512


def drawn_pair(key):
    key_queries, key_keys = jax.random.split(jax.random.fold_in(key, 11), 2)
    query_draw = jnp.clip(jax.random.normal(key_queries, (NCHUNK, ROWS, D), jnp.float32), -6.0, 6.0)
    key_draw = jnp.clip(jax.random.normal(key_keys, (NCHUNK, ROWS, KVD), jnp.float32), -6.0, 6.0)
    return (query_draw, key_draw)


def draw_queries(key, part):
    return drawn_pair(key)[0].astype(jnp.bfloat16)


def draw_keys(key, part):
    return drawn_pair(key)[1].astype(jnp.bfloat16)


def draw_block_mask(key, part):
    later = jnp.arange(NCHUNK)[:, None]
    earlier = jnp.arange(NCHUNK)[None, :]
    offset = later - earlier
    coins = jax.random.randint(jax.random.fold_in(key, 23), (NCHUNK, NCHUNK), 0, 2)
    inside = (offset >= 1) & (offset < WINDOW)
    return jnp.where(offset == 0, 1, jnp.where(inside, coins, 0)).astype(jnp.int32)


def shard_levels(stream_key, dims, shards, least, largest):
    level = 1.0
    for axis_at, shards_of in shards:
        steps = jax.random.uniform(jax.random.fold_in(jax.random.fold_in(stream_key, 6), axis_at), (shards_of,), jnp.float32, least / len(shards), largest / len(shards))
        level = level * jnp.repeat(jnp.exp(steps), dims[axis_at] // shards_of).reshape((-1,) + (1,) * (len(dims) - 1 - axis_at))
    return level


def profile(number_of, total, bound, skew):
    portions = [(1 << 20) // math.isqrt(standing ** skew) + 1 for standing in range(2, number_of + 1)]
    surplus, holding = total - bound - (number_of - 1), [1] * (number_of - 1)
    while surplus > 0:
        movable = [i for i in range(number_of - 1) if holding[i] < bound]
        pool, left = sum([portions[i] for i in movable]), surplus
        for i in movable:
            extra = min(bound - holding[i], max(1, left * portions[i] // pool), surplus)
            holding[i] = holding[i] + extra
            surplus = surplus - extra
    return np.array([bound] + holding)


def ragged_sizes(rng, amount, total, limit, skew):
    if amount == 2:
        one = jax.random.randint(rng, (), max(1, total - limit), min(limit, total - 1) + 1)
        return jnp.stack([one, total - one])
    lengths = jnp.asarray(profile(amount, total, limit, skew), jnp.int32)
    pairs = (amount - 1) // 2
    donor, receiver = lengths[1:1 + 2 * pairs:2], lengths[2:2 + 2 * pairs:2]
    room = jnp.minimum(donor - 1, limit - receiver)
    passed = jax.random.randint(jax.random.fold_in(rng, 1), (pairs,), 0, 1 << 20) % (room + 1)
    lengths = lengths.at[1:1 + 2 * pairs:2].set(donor - passed).at[2:2 + 2 * pairs:2].set(receiver + passed)
    return lengths[jax.random.permutation(jax.random.fold_in(rng, 2), amount)]


def noise(stream_key, shape, scale, reach, cuts=(), held_as=jnp.bfloat16):
    level = shard_levels(stream_key, shape, cuts, -0.22, 0.18) if cuts else 1.0
    result = jax.random.normal(stream_key, shape, jnp.float32) * scale * level
    return jnp.minimum(jnp.maximum(result, -reach), reach).astype(held_as)


def setup_inputs(seed: int = 0) -> dict:
    arg_keys = jax.random.split(jax.random.key(seed), 7)
    return {
        "queries": draw_queries(jax.random.fold_in(arg_keys[6], 71), 0),
        "keys": draw_keys(jax.random.fold_in(arg_keys[6], 71), 0),
        "values": noise(arg_keys[2], (NCHUNK, ROWS, KVD), 1.0, 6.0, ((0, 8), (1, 8))),
        "clip_ids": jnp.searchsorted(jnp.cumsum(ragged_sizes(arg_keys[3], CLIPS, ROWS, ROWS // 2, 2)), jnp.arange(ROWS), side="right").astype(jnp.int32),
        "block_mask": draw_block_mask(jax.random.fold_in(arg_keys[6], 71), 0),
        "out_weight": noise(arg_keys[5], (D, D), D ** -0.5, 0.078125, ((0, 12),)),
    }


def reference(queries, keys, values, clip_ids, block_mask, out_weight):
    score_scale = HEAD_DIM ** -0.5
    padding = WINDOW - 1
    padded_keys = jnp.concatenate([jnp.zeros((padding, ROWS, KVD), jnp.bfloat16), keys], axis=0)
    padded_values = jnp.concatenate([jnp.zeros((padding, ROWS, KVD), jnp.bfloat16), values], axis=0)
    padded_mask = jnp.concatenate([jnp.zeros((NCHUNK, padding), jnp.int32), block_mask], axis=1)
    same_clip = clip_ids[:, None] == clip_ids[None, :]

    def one_span(span_index):
        window_keys = lax.dynamic_slice_in_dim(padded_keys, span_index, WINDOW, 0).reshape(WINDOW * ROWS, KVD)
        window_values = lax.dynamic_slice_in_dim(padded_values, span_index, WINDOW, 0).reshape(WINDOW * ROWS, KVD)
        mask_row = lax.dynamic_index_in_dim(padded_mask, span_index, 0, keepdims=False)
        visible = lax.dynamic_slice_in_dim(mask_row, span_index, WINDOW, 0)
        allowed = (visible[:, None, None] == 1) & same_clip[None, :, :]
        allowed = jnp.transpose(allowed, (1, 0, 2)).reshape(ROWS, WINDOW * ROWS)
        span_queries = lax.dynamic_index_in_dim(queries, span_index, 0, keepdims=False)

        def head_out(head):
            start = (head * HEAD_DIM).astype(jnp.int32)
            kv_start = ((head // GROUP) * HEAD_DIM).astype(jnp.int32)
            query_head = lax.dynamic_slice_in_dim(span_queries, start, HEAD_DIM, 1)
            key_head = lax.dynamic_slice_in_dim(window_keys, kv_start, HEAD_DIM, 1)
            value_head = lax.dynamic_slice_in_dim(window_values, kv_start, HEAD_DIM, 1)
            s = jnp.dot(query_head, key_head.T, preferred_element_type=jnp.float32) * score_scale
            s = jnp.where(allowed, s, -jnp.inf)
            top = jnp.max(s, axis=1, keepdims=True)
            p = jnp.exp(s - top)
            total = jnp.sum(p, axis=1, keepdims=True)
            return jnp.dot(p.astype(jnp.bfloat16), value_head, preferred_element_type=jnp.float32) / total

        per_head = lax.map(head_out, jnp.arange(HEADS, dtype=jnp.int32))
        attended = jnp.transpose(per_head, (1, 0, 2)).reshape(ROWS, D).astype(jnp.bfloat16)
        return jnp.dot(attended, out_weight, preferred_element_type=jnp.float32).astype(jnp.bfloat16)

    return lax.map(one_span, jnp.arange(NCHUNK, dtype=jnp.int32))
```

```python
import jax
import jax.numpy as jnp
from jax import lax
from jax.sharding import PartitionSpec as P

HEAD_DIM = 128
WINDOW = 3
GROUP = 6
KV_SLOTS = 2


def passed_along(x, axis, by):
    size = lax.axis_size(axis)
    pairs = [(i, i + by) for i in range(size) if 0 <= i + by < size]
    return lax.ppermute(x, axis, pairs)


def on_device(queries, keys, values, clip_ids, block_mask, out_weight):
    row_count = queries.shape[1]
    local_width = queries.shape[2]
    head_count = local_width // HEAD_DIM
    kv_count = keys.shape[2] // HEAD_DIM
    score_scale = HEAD_DIM ** (-0.5)
    span_index = lax.axis_index("span")
    first_head = lax.axis_index("mp") * head_count
    first_kv = jnp.minimum(first_head // GROUP, kv_count - KV_SLOTS)
    kv_slot = (first_head + jnp.arange(head_count, dtype=jnp.int32)) // GROUP - first_kv
    kv_start = first_kv * HEAD_DIM
    slot_width = KV_SLOTS * HEAD_DIM
    own_keys = lax.dynamic_slice_in_dim(keys[0], kv_start, slot_width, 1)
    own_values = lax.dynamic_slice_in_dim(values[0], kv_start, slot_width, 1)
    packed = jnp.concatenate([own_keys, own_values], axis=1)
    mask_row = lax.dynamic_index_in_dim(block_mask, span_index, 0, keepdims=False)
    visible = []
    for j in range(WINDOW):
        earlier = span_index - j
        entry = lax.dynamic_index_in_dim(mask_row, jnp.maximum(earlier, 0), 0, keepdims=False)
        visible.append(jnp.where(earlier >= 0, entry, 0))
    stacked = [packed]
    for j in range(1, WINDOW):
        stacked.append(passed_along(packed, "span", j))
    blocks = lax.all_gather(jnp.stack(stacked, axis=0), "seq", axis=1, tiled=True)
    key_clips = lax.all_gather(clip_ids, "seq", axis=0, tiled=True)
    piece_rows = blocks.shape[1]
    window_rows = WINDOW * piece_rows
    kv = blocks.reshape(window_rows, 2, KV_SLOTS, HEAD_DIM)
    key_all = kv[:, 0]
    value_all = kv[:, 1]
    query_heads = queries[0].reshape(row_count, head_count, HEAD_DIM)
    s_both = jnp.einsum(
        "qhd,kad->ahqk", query_heads, key_all, preferred_element_type=jnp.float32
    )
    pick = kv_slot[:, None, None] == 0
    s = jnp.where(pick, s_both[0], s_both[1]) * score_scale
    span_ok = jnp.stack(visible) == 1
    allowed = span_ok[None, :, None] & (clip_ids[:, None, None] == key_clips[None, None, :])
    allowed = allowed.reshape(row_count, window_rows)
    s = jnp.where(allowed[None], s, -jnp.inf)
    top = jnp.max(s, axis=2, keepdims=True)
    p = jnp.exp(s - top)
    total = jnp.sum(p, axis=2, keepdims=True)
    acc_both = jnp.einsum(
        "hqk,kad->ahqd", p.astype(jnp.bfloat16), value_all, preferred_element_type=jnp.float32
    )
    acc = jnp.where(pick, acc_both[0], acc_both[1])
    attended = acc / total
    attended = (
        jnp.transpose(attended, (1, 0, 2)).reshape(row_count, local_width).astype(jnp.bfloat16)
    )
    partial_sum = jnp.dot(attended, out_weight, preferred_element_type=jnp.float32)[None]
    return lax.psum_scatter(partial_sum.astype(jnp.bfloat16), "mp", scatter_dimension=2, tiled=True)


def solution(mesh):
    in_specs = (
        P("span", "seq", "mp"),
        P("span", "seq", None),
        P("span", "seq", None),
        P("seq"),
        P(),
        P("mp", None),
    )
    out_specs = P("span", "seq", "mp")
    return jax.shard_map(
        on_device, mesh=mesh, in_specs=in_specs, out_specs=out_specs, check_vma=False
    )
```

```python
import jax
import jax.numpy as jnp
from jax import lax
from jax.sharding import PartitionSpec as P

HEAD_DIM = 128
WINDOW = 3
GROUP = 6
KV_SLOTS = 2
CLIP_PAD = 16


def passed_along(x, axis, by):
    size = lax.axis_size(axis)
    pairs = [(i, i + by) for i in range(size) if 0 <= i + by < size]
    return lax.ppermute(x, axis, pairs)


def on_device(queries, keys, values, clip_ids, block_mask, out_weight):
    row_count = queries.shape[1]
    local_width = queries.shape[2]
    head_count = local_width // HEAD_DIM
    kv_count = keys.shape[2] // HEAD_DIM
    score_scale = HEAD_DIM ** (-0.5)
    span_index = lax.axis_index("span")
    first_head = lax.axis_index("mp") * head_count
    first_kv = jnp.minimum(first_head // GROUP, kv_count - KV_SLOTS)
    kv_slot = (first_head + jnp.arange(head_count, dtype=jnp.int32)) // GROUP - first_kv
    kv_start = first_kv * HEAD_DIM
    slot_width = KV_SLOTS * HEAD_DIM
    own_keys = lax.dynamic_slice_in_dim(keys[0], kv_start, slot_width, 1)
    own_values = lax.dynamic_slice_in_dim(values[0], kv_start, slot_width, 1)
    packed = jnp.concatenate([own_keys, own_values], axis=1)
    mask_row = lax.dynamic_index_in_dim(block_mask, span_index, 0, keepdims=False)
    visible = []
    for j in range(WINDOW):
        earlier = span_index - j
        entry = lax.dynamic_index_in_dim(mask_row, jnp.maximum(earlier, 0), 0, keepdims=False)
        visible.append(jnp.where(earlier >= 0, entry, 0))
    stacked = [packed]
    for j in range(1, WINDOW):
        stacked.append(passed_along(packed, "span", j))
    clip_row = jnp.zeros((CLIP_PAD, packed.shape[1]), jnp.bfloat16)
    clip_row = clip_row.at[0, :row_count].set(clip_ids.astype(jnp.bfloat16))
    outgoing = jnp.concatenate(stacked + [clip_row], axis=0)
    seq_count = lax.axis_size("seq")
    outgoing = jnp.broadcast_to(outgoing[None], (seq_count,) + outgoing.shape)
    gathered = lax.all_to_all(outgoing, "seq", 0, 0, tiled=True)
    kv_rows = gathered[:, : WINDOW * row_count].reshape(seq_count, WINDOW, row_count, -1)
    key_clips = gathered[:, WINDOW * row_count, :row_count].reshape(-1)
    piece_rows = seq_count * row_count
    window_rows = WINDOW * piece_rows
    kv = jnp.transpose(kv_rows, (1, 0, 2, 3)).reshape(window_rows, 2, KV_SLOTS, HEAD_DIM)
    key_all = kv[:, 0]
    value_all = kv[:, 1]
    query_heads = queries[0].reshape(row_count, head_count, HEAD_DIM)
    s_both = jnp.einsum(
        "qhd,kad->ahqk", query_heads, key_all, preferred_element_type=jnp.float32
    )
    pick = kv_slot[:, None, None] == 0
    s = jnp.where(pick, s_both[0], s_both[1]) * score_scale
    span_ok = jnp.stack(visible) == 1
    query_clips = clip_ids.astype(jnp.bfloat16)
    allowed = span_ok[None, :, None] & (query_clips[:, None, None] == key_clips[None, None, :])
    allowed = allowed.reshape(row_count, window_rows)
    s = jnp.where(allowed[None], s, -jnp.inf)
    top = jnp.max(s, axis=2, keepdims=True)
    p = jnp.exp(s - top)
    total = jnp.sum(p, axis=2, keepdims=True)
    acc_both = jnp.einsum(
        "hqk,kad->ahqd", p.astype(jnp.bfloat16), value_all, preferred_element_type=jnp.float32
    )
    acc = jnp.where(pick, acc_both[0], acc_both[1])
    attended = acc / total
    attended = (
        jnp.transpose(attended, (1, 0, 2)).reshape(row_count, local_width).astype(jnp.bfloat16)
    )
    mp_count = lax.axis_size("mp")
    out_width = out_weight.shape[1] // mp_count
    weight_parts = out_weight.reshape(local_width, mp_count, out_width)
    partial_sum = jnp.einsum(
        "qi,icj->cqj", attended, weight_parts, preferred_element_type=jnp.float32
    ).astype(jnp.bfloat16)
    received = lax.all_to_all(partial_sum, "mp", 0, 0, tiled=True)
    projected = jnp.sum(received.astype(jnp.float32), axis=0)
    return projected.astype(jnp.bfloat16)[None]


def solution(mesh):
    in_specs = (
        P("span", "seq", "mp"),
        P("span", "seq", None),
        P("span", "seq", None),
        P("seq"),
        P(),
        P("mp", None),
    )
    out_specs = P("span", "seq", "mp")
    return jax.shard_map(
        on_device, mesh=mesh, in_specs=in_specs, out_specs=out_specs, check_vma=False
    )
```

```python
import jax
import jax.numpy as jnp
from jax import lax
from jax.sharding import PartitionSpec as P

HEAD_DIM = 128
WINDOW = 3
GROUP = 6
KV_SLOTS = 2
CLIP_PAD = 16


def passed_along(x, axis, by):
    size = lax.axis_size(axis)
    pairs = [(i, i + by) for i in range(size) if 0 <= i + by < size]
    return lax.ppermute(x, axis, pairs)


def on_device(queries, keys, values, clip_ids, block_mask, out_weight):
    row_count = queries.shape[1]
    local_width = queries.shape[2]
    head_count = local_width // HEAD_DIM
    kv_count = keys.shape[2] // HEAD_DIM
    score_scale = HEAD_DIM ** (-0.5)
    span_index = lax.axis_index("span")
    first_head = lax.axis_index("mp") * head_count
    first_kv = jnp.minimum(first_head // GROUP, kv_count - KV_SLOTS)
    kv_slot = (first_head + jnp.arange(head_count, dtype=jnp.int32)) // GROUP - first_kv
    kv_start = first_kv * HEAD_DIM
    slot_width = KV_SLOTS * HEAD_DIM
    own_keys = lax.dynamic_slice_in_dim(keys[0], kv_start, slot_width, 1)
    own_values = lax.dynamic_slice_in_dim(values[0], kv_start, slot_width, 1)
    packed = jnp.concatenate([own_keys, own_values], axis=1)
    mask_row = lax.dynamic_index_in_dim(block_mask, span_index, 0, keepdims=False)
    visible = []
    for j in range(WINDOW):
        earlier = span_index - j
        entry = lax.dynamic_index_in_dim(mask_row, jnp.maximum(earlier, 0), 0, keepdims=False)
        visible.append(jnp.where(earlier >= 0, entry, 0))
    stacked = [packed]
    for j in range(1, WINDOW):
        stacked.append(passed_along(packed, "span", j))
    clip_row = jnp.zeros((CLIP_PAD, packed.shape[1]), jnp.bfloat16)
    clip_row = clip_row.at[0, :row_count].set(clip_ids.astype(jnp.bfloat16))
    outgoing = jnp.concatenate(stacked + [clip_row], axis=0)
    seq_count = lax.axis_size("seq")
    held = [outgoing]
    for shift in range(2, seq_count, 2):
        pairs = [(i, (i + shift) % seq_count) for i in range(seq_count)]
        held.append(lax.ppermute(outgoing, "seq", pairs))
    held = jnp.stack(held, axis=0)
    partner = lax.ppermute(held, "seq", [(i, i ^ 1) for i in range(seq_count)])
    gathered = jnp.concatenate([held, partner], axis=0)
    kv_rows = gathered[:, : WINDOW * row_count].reshape(seq_count, WINDOW, row_count, -1)
    key_clips = gathered[:, WINDOW * row_count, :row_count].reshape(-1)
    piece_rows = seq_count * row_count
    window_rows = WINDOW * piece_rows
    kv = jnp.transpose(kv_rows, (1, 0, 2, 3)).reshape(window_rows, 2, KV_SLOTS, HEAD_DIM)
    key_all = kv[:, 0]
    value_all = kv[:, 1]
    query_heads = queries[0].reshape(row_count, head_count, HEAD_DIM)
    s_both = jnp.einsum(
        "qhd,kad->ahqk", query_heads, key_all, preferred_element_type=jnp.float32
    )
    pick = kv_slot[:, None, None] == 0
    s = jnp.where(pick, s_both[0], s_both[1]) * score_scale
    span_ok = jnp.stack(visible) == 1
    query_clips = clip_ids.astype(jnp.bfloat16)
    allowed = span_ok[None, :, None] & (query_clips[:, None, None] == key_clips[None, None, :])
    allowed = allowed.reshape(row_count, window_rows)
    s = jnp.where(allowed[None], s, -jnp.inf)
    top = jnp.max(s, axis=2, keepdims=True)
    p = jnp.exp(s - top)
    total = jnp.sum(p, axis=2, keepdims=True)
    acc_both = jnp.einsum(
        "hqk,kad->ahqd", p.astype(jnp.bfloat16), value_all, preferred_element_type=jnp.float32
    )
    acc = jnp.where(pick, acc_both[0], acc_both[1])
    attended = acc / total
    attended = (
        jnp.transpose(attended, (1, 0, 2)).reshape(row_count, local_width).astype(jnp.bfloat16)
    )
    mp_count = lax.axis_size("mp")
    out_width = out_weight.shape[1] // mp_count
    partial_sum = jnp.dot(attended, out_weight, preferred_element_type=jnp.float32)
    partial_sum = jnp.transpose(
        partial_sum.astype(jnp.bfloat16).reshape(row_count, mp_count, out_width), (1, 0, 2)
    )
    received = lax.all_to_all(partial_sum, "mp", 0, 0, tiled=True)
    projected = jnp.sum(received.astype(jnp.float32), axis=0)
    return projected.astype(jnp.bfloat16)[None]


def solution(mesh):
    in_specs = (
        P("span", "seq", "mp"),
        P("span", "seq", None),
        P("span", "seq", None),
        P("seq"),
        P(),
        P("mp", None),
    )
    out_specs = P("span", "seq", "mp")
    return jax.shard_map(
        on_device, mesh=mesh, in_specs=in_specs, out_specs=out_specs, check_vma=False
    )
```

```python
import jax
import jax.numpy as jnp
from jax import lax
from jax.sharding import PartitionSpec as P

HEAD_DIM = 128
WINDOW = 3
GROUP = 6
KV_SLOTS = 2
CLIP_PAD = 16


def passed_along(x, axis, by):
    size = lax.axis_size(axis)
    pairs = [(i, i + by) for i in range(size) if 0 <= i + by < size]
    return lax.ppermute(x, axis, pairs)


def on_device(queries, keys, values, clip_ids, block_mask, out_weight):
    row_count = queries.shape[1]
    local_width = queries.shape[2]
    head_count = local_width // HEAD_DIM
    kv_count = keys.shape[2] // HEAD_DIM
    score_scale = HEAD_DIM ** (-0.5)
    span_index = lax.axis_index("span")
    first_head = lax.axis_index("mp") * head_count
    first_kv = jnp.minimum(first_head // GROUP, kv_count - KV_SLOTS)
    kv_slot = (first_head + jnp.arange(head_count, dtype=jnp.int32)) // GROUP - first_kv
    kv_start = first_kv * HEAD_DIM
    slot_width = KV_SLOTS * HEAD_DIM
    own_keys = lax.dynamic_slice_in_dim(keys[0], kv_start, slot_width, 1)
    own_values = lax.dynamic_slice_in_dim(values[0], kv_start, slot_width, 1)
    packed = jnp.concatenate([own_keys, own_values], axis=1)
    mask_row = lax.dynamic_index_in_dim(block_mask, span_index, 0, keepdims=False)
    visible = []
    for j in range(WINDOW):
        earlier = span_index - j
        entry = lax.dynamic_index_in_dim(mask_row, jnp.maximum(earlier, 0), 0, keepdims=False)
        visible.append(jnp.where(earlier >= 0, entry, 0))
    stacked = [packed]
    for j in range(1, WINDOW):
        stacked.append(passed_along(packed, "span", j))
    clip_row = jnp.zeros((CLIP_PAD, packed.shape[1]), jnp.bfloat16)
    clip_row = clip_row.at[0, :row_count].set(clip_ids.astype(jnp.bfloat16))
    outgoing = jnp.concatenate(stacked + [clip_row], axis=0)
    seq_count = lax.axis_size("seq")
    held = [outgoing]
    for shift in range(2, seq_count, 2):
        pairs = [(i, (i + shift) % seq_count) for i in range(seq_count)]
        held.append(lax.ppermute(outgoing, "seq", pairs))
    held = jnp.stack(held, axis=0)
    partner = lax.ppermute(held, "seq", [(i, i ^ 1) for i in range(seq_count)])
    gathered = jnp.concatenate([held, partner], axis=0)
    kv_rows = gathered[:, : WINDOW * row_count].reshape(seq_count, WINDOW, row_count, -1)
    key_clips = gathered[:, WINDOW * row_count, :row_count].reshape(-1)
    piece_rows = seq_count * row_count
    window_rows = WINDOW * piece_rows
    kv = jnp.transpose(kv_rows, (1, 0, 2, 3)).reshape(window_rows, 2, KV_SLOTS, HEAD_DIM)
    key_all = kv[:, 0]
    value_all = kv[:, 1]
    query_heads = queries[0].reshape(row_count, head_count, HEAD_DIM)
    s_both = jnp.einsum(
        "qhd,kad->ahqk", query_heads, key_all, preferred_element_type=jnp.float32
    )
    pick = kv_slot[:, None, None] == 0
    s = jnp.where(pick, s_both[0], s_both[1]) * score_scale
    span_ok = jnp.stack(visible) == 1
    query_clips = clip_ids.astype(jnp.bfloat16)
    allowed = span_ok[None, :, None] & (query_clips[:, None, None] == key_clips[None, None, :])
    allowed = allowed.reshape(row_count, window_rows)
    s = jnp.where(allowed[None], s, -jnp.inf)
    top = jnp.max(s, axis=2, keepdims=True)
    p = jnp.exp(s - top)
    total = jnp.sum(p, axis=2, keepdims=True)
    acc_both = jnp.einsum(
        "hqk,kad->ahqd", p.astype(jnp.bfloat16), value_all, preferred_element_type=jnp.float32
    )
    acc = jnp.where(pick, acc_both[0], acc_both[1])
    attended = acc / total
    attended = (
        jnp.transpose(attended, (1, 0, 2)).reshape(row_count, local_width).astype(jnp.bfloat16)
    )
    mp_count = lax.axis_size("mp")
    out_width = out_weight.shape[1] // mp_count
    partial_sum = jnp.dot(attended, out_weight, preferred_element_type=jnp.float32)
    partial_sum = partial_sum.reshape(row_count, mp_count, out_width)
    trio = 3
    trios = mp_count // trio
    place = lax.axis_index("mp") % trio
    by_trio = jnp.transpose(
        partial_sum.reshape(row_count, trios, trio, out_width), (2, 1, 0, 3)
    ).astype(jnp.bfloat16)
    summed = lax.dynamic_index_in_dim(by_trio, place, 0, keepdims=False).astype(jnp.float32)
    for step in range(1, trio):
        pairs = [(i, trio * (i // trio) + (i % trio + step) % trio) for i in range(mp_count)]
        target = (place + step) % trio
        sent = lax.dynamic_index_in_dim(by_trio, target, 0, keepdims=False)
        summed = summed + lax.ppermute(sent, "mp", pairs).astype(jnp.float32)
    partial_trio = summed.astype(jnp.bfloat16)
    group = lax.axis_index("mp") // trio
    total_sum = lax.dynamic_index_in_dim(partial_trio, group, 0, keepdims=False).astype(jnp.float32)
    for step in range(1, trios):
        pairs = [(i, (i + trio * step) % mp_count) for i in range(mp_count)]
        target = (group + step) % trios
        sent = lax.dynamic_index_in_dim(partial_trio, target, 0, keepdims=False)
        total_sum = total_sum + lax.ppermute(sent, "mp", pairs).astype(jnp.float32)
    return total_sum.astype(jnp.bfloat16)[None]


def solution(mesh):
    in_specs = (
        P("span", "seq", "mp"),
        P("span", "seq", None),
        P("span", "seq", None),
        P("seq"),
        P(),
        P("mp", None),
    )
    out_specs = P("span", "seq", "mp")
    return jax.shard_map(
        on_device, mesh=mesh, in_specs=in_specs, out_specs=out_specs, check_vma=False
    )
```

```python
import jax
import jax.numpy as jnp
from jax import lax
from jax.sharding import PartitionSpec as P

HEAD_DIM = 128
WINDOW = 3
GROUP = 6
LENT_HEADS = 2
CLIP_PAD = 16


def passed_along(x, axis, by):
    size = lax.axis_size(axis)
    pairs = [(i, i + by) for i in range(size) if 0 <= i + by < size]
    return lax.ppermute(x, axis, pairs)


def lending_pairs(mp_count, head_count, lent):
    pairs = []
    for i in range(mp_count):
        groups = [(i * head_count + h) // GROUP for h in range(head_count)]
        if len(set(groups)) == 1:
            continue
        assert len(set(groups[:lent])) == 1 and len(set(groups[lent:])) == 1
        assert i + 1 < mp_count and groups[lent] == ((i + 1) * head_count) // GROUP
        pairs.append((i, i + 1))
    return pairs


def on_device(queries, keys, values, clip_ids, block_mask, out_weight):
    row_count = queries.shape[1]
    local_width = queries.shape[2]
    head_count = local_width // HEAD_DIM
    kv_count = keys.shape[2] // HEAD_DIM
    score_scale = HEAD_DIM ** (-0.5)
    span_index = lax.axis_index("span")
    first_head = lax.axis_index("mp") * head_count
    mp_index = lax.axis_index("mp")
    mp_count = lax.axis_size("mp")
    kv_start = (first_head // GROUP) * HEAD_DIM
    own_keys = lax.dynamic_slice_in_dim(keys[0], kv_start, HEAD_DIM, 1)
    own_values = lax.dynamic_slice_in_dim(values[0], kv_start, HEAD_DIM, 1)
    packed = jnp.concatenate([own_keys, own_values], axis=1)
    lent = head_count - LENT_HEADS
    lends = lending_pairs(mp_count, head_count, lent)
    borrowed = lax.ppermute(queries[0][:, lent * HEAD_DIM :], "mp", lends)
    lender = jnp.zeros((), jnp.bool_)
    for i, _ in lends:
        lender = lender | (mp_index == i)
    mask_row = lax.dynamic_index_in_dim(block_mask, span_index, 0, keepdims=False)
    visible = []
    for j in range(WINDOW):
        earlier = span_index - j
        entry = lax.dynamic_index_in_dim(mask_row, jnp.maximum(earlier, 0), 0, keepdims=False)
        visible.append(jnp.where(earlier >= 0, entry, 0))
    stacked = [packed]
    for j in range(1, WINDOW):
        stacked.append(passed_along(packed, "span", j))
    clip_row = jnp.zeros((CLIP_PAD, packed.shape[1]), jnp.bfloat16)
    clip_row = clip_row.at[0, :row_count].set(clip_ids.astype(jnp.bfloat16))
    outgoing = jnp.concatenate(stacked + [clip_row], axis=0)
    seq_count = lax.axis_size("seq")
    held = [outgoing]
    for shift in range(2, seq_count, 2):
        pairs = [(i, (i + shift) % seq_count) for i in range(seq_count)]
        held.append(lax.ppermute(outgoing, "seq", pairs))
    held = jnp.stack(held, axis=0)
    partner = lax.ppermute(held, "seq", [(i, i ^ 1) for i in range(seq_count)])
    gathered = jnp.concatenate([held, partner], axis=0)
    kv_rows = gathered[:, : WINDOW * row_count].reshape(seq_count, WINDOW, row_count, -1)
    key_clips = gathered[:, WINDOW * row_count, :row_count].reshape(-1)
    piece_rows = seq_count * row_count
    window_rows = WINDOW * piece_rows
    kv = jnp.transpose(kv_rows, (1, 0, 2, 3)).reshape(window_rows, 2, HEAD_DIM)
    key_all = kv[:, 0]
    value_all = kv[:, 1]
    all_queries = jnp.concatenate([queries[0], borrowed], axis=1)
    query_heads = all_queries.reshape(row_count, head_count + LENT_HEADS, HEAD_DIM)
    s = jnp.einsum("qhd,kd->hqk", query_heads, key_all, preferred_element_type=jnp.float32)
    s = s * score_scale
    span_ok = jnp.stack(visible) == 1
    query_clips = clip_ids.astype(jnp.bfloat16)
    allowed = span_ok[None, :, None] & (query_clips[:, None, None] == key_clips[None, None, :])
    allowed = allowed.reshape(row_count, window_rows)
    s = jnp.where(allowed[None], s, -jnp.inf)
    top = jnp.max(s, axis=2, keepdims=True)
    p = jnp.exp(s - top)
    total = jnp.sum(p, axis=2, keepdims=True)
    acc = jnp.einsum(
        "hqk,kd->hqd", p.astype(jnp.bfloat16), value_all, preferred_element_type=jnp.float32
    )
    attended = (acc / total).astype(jnp.bfloat16)
    returned = lax.ppermute(attended[head_count:], "mp", [(j, i) for i, j in lends])
    mine = attended[:head_count]
    mine = jnp.concatenate([mine[:lent], jnp.where(lender, returned, mine[lent:])], axis=0)
    attended = jnp.transpose(mine, (1, 0, 2)).reshape(row_count, local_width)
    out_width = out_weight.shape[1] // mp_count
    partial_sum = jnp.dot(attended, out_weight, preferred_element_type=jnp.float32)
    partial_sum = jnp.transpose(
        partial_sum.astype(jnp.bfloat16).reshape(row_count, mp_count, out_width), (1, 0, 2)
    )
    received = lax.all_to_all(partial_sum, "mp", 0, 0, tiled=True)
    projected = jnp.sum(received.astype(jnp.float32), axis=0)
    return projected.astype(jnp.bfloat16)[None]


def solution(mesh):
    in_specs = (
        P("span", "seq", "mp"),
        P("span", "seq", None),
        P("span", "seq", None),
        P("seq"),
        P(),
        P("mp", None),
    )
    out_specs = P("span", "seq", "mp")
    return jax.shard_map(
        on_device, mesh=mesh, in_specs=in_specs, out_specs=out_specs, check_vma=False
    )
```

```python
import jax
import jax.numpy as jnp
from jax import lax
from jax.sharding import PartitionSpec as P

HEAD_DIM = 128
WINDOW = 3
GROUP = 6
KV_SLOTS = 2
CLIP_PAD = 16


def passed_along(x, axis, by):
    size = lax.axis_size(axis)
    pairs = [(i, i + by) for i in range(size) if 0 <= i + by < size]
    return lax.ppermute(x, axis, pairs)


def on_device(queries, keys, values, clip_ids, block_mask, out_weight):
    row_count = queries.shape[1]
    local_width = queries.shape[2]
    head_count = local_width // HEAD_DIM
    kv_count = keys.shape[2] // HEAD_DIM
    score_scale = HEAD_DIM ** (-0.5)
    span_index = lax.axis_index("span")
    trio = lax.axis_size("mp_lo")
    first_head = (lax.axis_index("mp_hi") * trio + lax.axis_index("mp_lo")) * head_count
    first_kv = jnp.minimum(first_head // GROUP, kv_count - KV_SLOTS)
    kv_slot = (first_head + jnp.arange(head_count, dtype=jnp.int32)) // GROUP - first_kv
    kv_start = first_kv * HEAD_DIM
    slot_width = KV_SLOTS * HEAD_DIM
    own_keys = lax.dynamic_slice_in_dim(keys[0], kv_start, slot_width, 1)
    own_values = lax.dynamic_slice_in_dim(values[0], kv_start, slot_width, 1)
    packed = jnp.concatenate([own_keys, own_values], axis=1)
    mask_row = lax.dynamic_index_in_dim(block_mask, span_index, 0, keepdims=False)
    visible = []
    for j in range(WINDOW):
        earlier = span_index - j
        entry = lax.dynamic_index_in_dim(mask_row, jnp.maximum(earlier, 0), 0, keepdims=False)
        visible.append(jnp.where(earlier >= 0, entry, 0))
    stacked = [packed]
    for j in range(1, WINDOW):
        stacked.append(passed_along(packed, "span", j))
    clip_row = jnp.zeros((CLIP_PAD, packed.shape[1]), jnp.bfloat16)
    clip_row = clip_row.at[0, :row_count].set(clip_ids.astype(jnp.bfloat16))
    outgoing = jnp.concatenate(stacked + [clip_row], axis=0)
    seq_count = lax.axis_size("seq")
    held = [outgoing]
    for shift in range(2, seq_count, 2):
        pairs = [(i, (i + shift) % seq_count) for i in range(seq_count)]
        held.append(lax.ppermute(outgoing, "seq", pairs))
    held = jnp.stack(held, axis=0)
    partner = lax.ppermute(held, "seq", [(i, i ^ 1) for i in range(seq_count)])
    gathered = jnp.concatenate([held, partner], axis=0)
    kv_rows = gathered[:, : WINDOW * row_count].reshape(seq_count, WINDOW, row_count, -1)
    key_clips = gathered[:, WINDOW * row_count, :row_count].reshape(-1)
    piece_rows = seq_count * row_count
    window_rows = WINDOW * piece_rows
    kv = jnp.transpose(kv_rows, (1, 0, 2, 3)).reshape(window_rows, 2, KV_SLOTS, HEAD_DIM)
    key_all = kv[:, 0]
    value_all = kv[:, 1]
    query_heads = queries[0].reshape(row_count, head_count, HEAD_DIM)
    s_both = jnp.einsum(
        "qhd,kad->ahqk", query_heads, key_all, preferred_element_type=jnp.float32
    )
    pick = kv_slot[:, None, None] == 0
    s = jnp.where(pick, s_both[0], s_both[1]) * score_scale
    span_ok = jnp.stack(visible) == 1
    query_clips = clip_ids.astype(jnp.bfloat16)
    allowed = span_ok[None, :, None] & (query_clips[:, None, None] == key_clips[None, None, :])
    allowed = allowed.reshape(row_count, window_rows)
    s = jnp.where(allowed[None], s, -jnp.inf)
    top = jnp.max(s, axis=2, keepdims=True)
    p = jnp.exp(s - top)
    total = jnp.sum(p, axis=2, keepdims=True)
    acc_both = jnp.einsum(
        "hqk,kad->ahqd", p.astype(jnp.bfloat16), value_all, preferred_element_type=jnp.float32
    )
    acc = jnp.where(pick, acc_both[0], acc_both[1])
    attended = acc / total
    attended = (
        jnp.transpose(attended, (1, 0, 2)).reshape(row_count, local_width).astype(jnp.bfloat16)
    )
    trios = lax.axis_size("mp_hi")
    out_width = out_weight.shape[1] // (trios * trio)
    partial_sum = jnp.dot(attended, out_weight, preferred_element_type=jnp.float32)
    partial_sum = jnp.transpose(
        partial_sum.astype(jnp.bfloat16).reshape(row_count, trios, trio, out_width), (2, 1, 0, 3)
    )
    received = lax.all_to_all(partial_sum, "mp_lo", 0, 0, tiled=True)
    partial_trio = jnp.sum(received.astype(jnp.float32), axis=0).astype(jnp.bfloat16)
    received = lax.all_to_all(partial_trio, "mp_hi", 0, 0, tiled=True)
    projected = jnp.sum(received.astype(jnp.float32), axis=0)
    return projected.astype(jnp.bfloat16)[None]


def solution(mesh):
    shape = dict(mesh.shape)
    trio = 3
    split = jax.sharding.Mesh(
        mesh.devices.reshape(shape["span"], shape["seq"], shape["mp"] // trio, trio),
        ("span", "seq", "mp_hi", "mp_lo"),
    )
    mp = ("mp_hi", "mp_lo")
    in_specs = (
        P("span", "seq", mp),
        P("span", "seq", None),
        P("span", "seq", None),
        P("seq"),
        P(),
        P(mp, None),
    )
    out_specs = P("span", "seq", mp)
    return jax.shard_map(
        on_device, mesh=split, in_specs=in_specs, out_specs=out_specs, check_vma=False
    )
```

```python
import jax
import jax.numpy as jnp
from jax import lax
from jax.sharding import PartitionSpec as P

HEAD_DIM = 128
WINDOW = 3
GROUP = 6
KV_SLOTS = 2
CLIP_PAD = 16


def passed_along(x, axis, by):
    size = lax.axis_size(axis)
    pairs = [(i, i + by) for i in range(size) if 0 <= i + by < size]
    return lax.ppermute(x, axis, pairs)


def on_device(queries, keys, values, clip_ids, block_mask, out_weight):
    row_count = queries.shape[1]
    local_width = queries.shape[2]
    head_count = local_width // HEAD_DIM
    kv_count = keys.shape[2] // HEAD_DIM
    score_scale = HEAD_DIM ** (-0.5)
    span_index = lax.axis_index("span")
    first_head = lax.axis_index("mp") * head_count
    first_kv = jnp.minimum(first_head // GROUP, kv_count - KV_SLOTS)
    kv_slot = (first_head + jnp.arange(head_count, dtype=jnp.int32)) // GROUP - first_kv
    kv_start = first_kv * HEAD_DIM
    slot_width = KV_SLOTS * HEAD_DIM
    own_keys = lax.dynamic_slice_in_dim(keys[0], kv_start, slot_width, 1)
    own_values = lax.dynamic_slice_in_dim(values[0], kv_start, slot_width, 1)
    packed = jnp.concatenate([own_keys, own_values], axis=1)
    mask_row = lax.dynamic_index_in_dim(block_mask, span_index, 0, keepdims=False)
    visible = []
    for j in range(WINDOW):
        earlier = span_index - j
        entry = lax.dynamic_index_in_dim(mask_row, jnp.maximum(earlier, 0), 0, keepdims=False)
        visible.append(jnp.where(earlier >= 0, entry, 0))
    clip_row = jnp.zeros((CLIP_PAD, packed.shape[1]), jnp.bfloat16)
    clip_row = clip_row.at[0, :row_count].set(clip_ids.astype(jnp.bfloat16))
    outgoing = jnp.concatenate([packed, clip_row], axis=0)
    span_count = lax.axis_size("span")
    seq_count = lax.axis_size("seq")
    held = []
    for j in range(WINDOW):
        for shift in range(0, seq_count, 2):
            if j == 0 and shift == 0:
                held.append(outgoing)
                continue
            pairs = [
                (c * seq_count + s, (c + j) * seq_count + (s + shift) % seq_count)
                for c in range(span_count - j)
                for s in range(seq_count)
            ]
            held.append(lax.ppermute(outgoing, ("span", "seq"), pairs))
    held = jnp.stack(held, axis=0).reshape(WINDOW, seq_count // 2, *outgoing.shape)
    partner = lax.ppermute(held, "seq", [(i, i ^ 1) for i in range(seq_count)])
    gathered = jnp.concatenate([held, partner], axis=1)
    key_clips = gathered[0, :, row_count, :row_count].reshape(-1)
    window_rows = WINDOW * seq_count * row_count
    kv = gathered[:, :, :row_count].reshape(window_rows, 2, KV_SLOTS, HEAD_DIM)
    key_all = kv[:, 0]
    value_all = kv[:, 1]
    query_heads = queries[0].reshape(row_count, head_count, HEAD_DIM)
    s_both = jnp.einsum(
        "qhd,kad->ahqk", query_heads, key_all, preferred_element_type=jnp.float32
    )
    pick = kv_slot[:, None, None] == 0
    s = jnp.where(pick, s_both[0], s_both[1]) * score_scale
    span_ok = jnp.stack(visible) == 1
    query_clips = clip_ids.astype(jnp.bfloat16)
    allowed = span_ok[None, :, None] & (query_clips[:, None, None] == key_clips[None, None, :])
    allowed = allowed.reshape(row_count, window_rows)
    s = jnp.where(allowed[None], s, -jnp.inf)
    top = jnp.max(s, axis=2, keepdims=True)
    p = jnp.exp(s - top)
    total = jnp.sum(p, axis=2, keepdims=True)
    acc_both = jnp.einsum(
        "hqk,kad->ahqd", p.astype(jnp.bfloat16), value_all, preferred_element_type=jnp.float32
    )
    acc = jnp.where(pick, acc_both[0], acc_both[1])
    attended = acc / total
    attended = (
        jnp.transpose(attended, (1, 0, 2)).reshape(row_count, local_width).astype(jnp.bfloat16)
    )
    mp_count = lax.axis_size("mp")
    out_width = out_weight.shape[1] // mp_count
    partial_sum = jnp.dot(attended, out_weight, preferred_element_type=jnp.float32)
    partial_sum = jnp.transpose(
        partial_sum.astype(jnp.bfloat16).reshape(row_count, mp_count, out_width), (1, 0, 2)
    )
    received = lax.all_to_all(partial_sum, "mp", 0, 0, tiled=True)
    projected = jnp.sum(received.astype(jnp.float32), axis=0)
    return projected.astype(jnp.bfloat16)[None]


def solution(mesh):
    in_specs = (
        P("span", "seq", "mp"),
        P("span", "seq", None),
        P("span", "seq", None),
        P("seq"),
        P(),
        P("mp", None),
    )
    out_specs = P("span", "seq", "mp")
    return jax.shard_map(
        on_device, mesh=mesh, in_specs=in_specs, out_specs=out_specs, check_vma=False
    )
```

```python
import jax
import jax.numpy as jnp
from jax import lax
from jax.sharding import PartitionSpec as P

HEAD_DIM = 128
WINDOW = 3
GROUP = 6
KV_SLOTS = 2
CLIP_PAD = 16


def passed_along(x, axis, by):
    size = lax.axis_size(axis)
    pairs = [(i, i + by) for i in range(size) if 0 <= i + by < size]
    return lax.ppermute(x, axis, pairs)


def on_device(queries, keys, values, clip_ids, block_mask, out_weight):
    row_count = queries.shape[1]
    local_width = queries.shape[2]
    head_count = local_width // HEAD_DIM
    kv_count = keys.shape[2] // HEAD_DIM
    score_scale = HEAD_DIM ** (-0.5)
    span_index = lax.axis_index("span")
    first_head = lax.axis_index("mp") * head_count
    first_kv = jnp.minimum(first_head // GROUP, kv_count - KV_SLOTS)
    kv_slot = (first_head + jnp.arange(head_count, dtype=jnp.int32)) // GROUP - first_kv
    kv_start = first_kv * HEAD_DIM
    slot_width = KV_SLOTS * HEAD_DIM
    own_keys = lax.dynamic_slice_in_dim(keys[0], kv_start, slot_width, 1)
    own_values = lax.dynamic_slice_in_dim(values[0], kv_start, slot_width, 1)
    packed = jnp.concatenate([own_keys, own_values], axis=1)
    mask_row = lax.dynamic_index_in_dim(block_mask, span_index, 0, keepdims=False)
    visible = []
    for j in range(WINDOW):
        earlier = span_index - j
        entry = lax.dynamic_index_in_dim(mask_row, jnp.maximum(earlier, 0), 0, keepdims=False)
        visible.append(jnp.where(earlier >= 0, entry, 0))
    stacked = [packed]
    for j in range(1, WINDOW):
        stacked.append(passed_along(packed, "span", j))
    clip_row = jnp.zeros((CLIP_PAD, packed.shape[1]), jnp.bfloat16)
    clip_row = clip_row.at[0, :row_count].set(clip_ids.astype(jnp.bfloat16))
    outgoing = jnp.concatenate(stacked + [clip_row], axis=0)
    seq_count = lax.axis_size("seq")
    held = [outgoing]
    for shift in range(2, seq_count, 2):
        pairs = [(i, (i + shift) % seq_count) for i in range(seq_count)]
        held.append(lax.ppermute(outgoing, "seq", pairs))
    held = jnp.stack(held, axis=0)
    partner = lax.ppermute(held, "seq", [(i, i ^ 1) for i in range(seq_count)])
    query_heads = queries[0].reshape(row_count, head_count, HEAD_DIM)
    pick = kv_slot[:, None, None] == 0
    span_ok = jnp.stack(visible) == 1
    query_clips = clip_ids.astype(jnp.bfloat16)

    def piece_scores(piece):
        blocks = piece.shape[0]
        kv_rows = piece[:, : WINDOW * row_count].reshape(blocks, WINDOW, row_count, -1)
        key_clips = piece[:, WINDOW * row_count, :row_count].reshape(-1)
        rows = WINDOW * blocks * row_count
        kv = jnp.transpose(kv_rows, (1, 0, 2, 3)).reshape(rows, 2, KV_SLOTS, HEAD_DIM)
        s_both = jnp.einsum(
            "qhd,kad->ahqk", query_heads, kv[:, 0], preferred_element_type=jnp.float32
        )
        s = jnp.where(pick, s_both[0], s_both[1]) * score_scale
        same = query_clips[:, None, None] == key_clips[None, None, :]
        allowed = (span_ok[None, :, None] & same).reshape(row_count, rows)
        return jnp.where(allowed[None], s, -jnp.inf), kv[:, 1]

    def weighted(p, value_all):
        acc_both = jnp.einsum(
            "hqk,kad->ahqd", p.astype(jnp.bfloat16), value_all, preferred_element_type=jnp.float32
        )
        return jnp.where(pick, acc_both[0], acc_both[1])

    s, value_all = piece_scores(held)
    first_top = jnp.max(s, axis=2, keepdims=True)
    p = jnp.exp(s - first_top)
    first_total = jnp.sum(p, axis=2, keepdims=True)
    first_acc = weighted(p, value_all)
    s, value_all = piece_scores(partner)
    top = jnp.maximum(first_top, jnp.max(s, axis=2, keepdims=True))
    p = jnp.exp(s - top)
    factor = jnp.exp(first_top - top)
    total = first_total * factor + jnp.sum(p, axis=2, keepdims=True)
    acc = first_acc * factor + weighted(p, value_all)
    attended = acc / total
    attended = (
        jnp.transpose(attended, (1, 0, 2)).reshape(row_count, local_width).astype(jnp.bfloat16)
    )
    mp_count = lax.axis_size("mp")
    out_width = out_weight.shape[1] // mp_count
    partial_sum = jnp.dot(attended, out_weight, preferred_element_type=jnp.float32)
    partial_sum = jnp.transpose(
        partial_sum.astype(jnp.bfloat16).reshape(row_count, mp_count, out_width), (1, 0, 2)
    )
    received = lax.all_to_all(partial_sum, "mp", 0, 0, tiled=True)
    projected = jnp.sum(received.astype(jnp.float32), axis=0)
    return projected.astype(jnp.bfloat16)[None]


def solution(mesh):
    in_specs = (
        P("span", "seq", "mp"),
        P("span", "seq", None),
        P("span", "seq", None),
        P("seq"),
        P(),
        P("mp", None),
    )
    out_specs = P("span", "seq", "mp")
    return jax.shard_map(
        on_device, mesh=mesh, in_specs=in_specs, out_specs=out_specs, check_vma=False
    )
```

```python
import jax
import jax.numpy as jnp
from jax import lax
from jax.sharding import PartitionSpec as P

HEAD_DIM = 128
WINDOW = 3
GROUP = 6
KV_SLOTS = 2
CLIP_PAD = 16


def passed_along(x, axis, by):
    size = lax.axis_size(axis)
    pairs = [(i, i + by) for i in range(size) if 0 <= i + by < size]
    return lax.ppermute(x, axis, pairs)


def on_device(queries, keys, values, clip_ids, block_mask, out_weight):
    row_count = queries.shape[1]
    local_width = queries.shape[2]
    head_count = local_width // HEAD_DIM
    kv_count = keys.shape[2] // HEAD_DIM
    score_scale = HEAD_DIM ** (-0.5)
    span_index = lax.axis_index("span")
    trio = lax.axis_size("mp_lo")
    first_head = (lax.axis_index("mp_hi") * trio + lax.axis_index("mp_lo")) * head_count
    first_kv = jnp.minimum(first_head // GROUP, kv_count - KV_SLOTS)
    kv_slot = (first_head + jnp.arange(head_count, dtype=jnp.int32)) // GROUP - first_kv
    kv_start = first_kv * HEAD_DIM
    slot_width = KV_SLOTS * HEAD_DIM
    own_keys = lax.dynamic_slice_in_dim(keys[0], kv_start, slot_width, 1)
    own_values = lax.dynamic_slice_in_dim(values[0], kv_start, slot_width, 1)
    packed = jnp.concatenate([own_keys, own_values], axis=1)
    mask_row = lax.dynamic_index_in_dim(block_mask, span_index, 0, keepdims=False)
    visible = []
    for j in range(WINDOW):
        earlier = span_index - j
        entry = lax.dynamic_index_in_dim(mask_row, jnp.maximum(earlier, 0), 0, keepdims=False)
        visible.append(jnp.where(earlier >= 0, entry, 0))
    stacked = [packed]
    for j in range(1, WINDOW):
        stacked.append(passed_along(packed, "span", j))
    clip_row = jnp.zeros((CLIP_PAD, packed.shape[1]), jnp.bfloat16)
    clip_row = clip_row.at[0, :row_count].set(clip_ids.astype(jnp.bfloat16))
    outgoing = jnp.concatenate(stacked + [clip_row], axis=0)
    seq_count = lax.axis_size("seq")
    held = [outgoing]
    for shift in range(2, seq_count, 2):
        pairs = [(i, (i + shift) % seq_count) for i in range(seq_count)]
        held.append(lax.ppermute(outgoing, "seq", pairs))
    held = jnp.stack(held, axis=0)
    partner = lax.ppermute(held, "seq", [(i, i ^ 1) for i in range(seq_count)])
    query_heads = queries[0].reshape(row_count, head_count, HEAD_DIM)
    pick = kv_slot[:, None, None] == 0
    span_ok = jnp.stack(visible) == 1
    query_clips = clip_ids.astype(jnp.bfloat16)

    def piece_scores(piece):
        blocks = piece.shape[0]
        kv_rows = piece[:, : WINDOW * row_count].reshape(blocks, WINDOW, row_count, -1)
        key_clips = piece[:, WINDOW * row_count, :row_count].reshape(-1)
        rows = WINDOW * blocks * row_count
        kv = jnp.transpose(kv_rows, (1, 0, 2, 3)).reshape(rows, 2, KV_SLOTS, HEAD_DIM)
        s_both = jnp.einsum(
            "qhd,kad->ahqk", query_heads, kv[:, 0], preferred_element_type=jnp.float32
        )
        s = jnp.where(pick, s_both[0], s_both[1]) * score_scale
        same = query_clips[:, None, None] == key_clips[None, None, :]
        allowed = (span_ok[None, :, None] & same).reshape(row_count, rows)
        return jnp.where(allowed[None], s, -jnp.inf), kv[:, 1]

    def weighted(p, value_all):
        acc_both = jnp.einsum(
            "hqk,kad->ahqd", p.astype(jnp.bfloat16), value_all, preferred_element_type=jnp.float32
        )
        return jnp.where(pick, acc_both[0], acc_both[1])

    s, value_all = piece_scores(held)
    first_top = jnp.max(s, axis=2, keepdims=True)
    p = jnp.exp(s - first_top)
    first_total = jnp.sum(p, axis=2, keepdims=True)
    first_acc = weighted(p, value_all)
    s, value_all = piece_scores(partner)
    top = jnp.maximum(first_top, jnp.max(s, axis=2, keepdims=True))
    p = jnp.exp(s - top)
    factor = jnp.exp(first_top - top)
    total = first_total * factor + jnp.sum(p, axis=2, keepdims=True)
    acc = first_acc * factor + weighted(p, value_all)
    attended = acc / total
    attended = (
        jnp.transpose(attended, (1, 0, 2)).reshape(row_count, local_width).astype(jnp.bfloat16)
    )
    trios = lax.axis_size("mp_hi")
    out_width = out_weight.shape[1] // (trios * trio)
    partial_sum = jnp.dot(attended, out_weight, preferred_element_type=jnp.float32)
    partial_sum = jnp.transpose(
        partial_sum.astype(jnp.bfloat16).reshape(row_count, trios, trio, out_width), (2, 1, 0, 3)
    )
    received = lax.all_to_all(partial_sum, "mp_lo", 0, 0, tiled=True)
    partial_trio = jnp.sum(received.astype(jnp.float32), axis=0).astype(jnp.bfloat16)
    received = lax.all_to_all(partial_trio, "mp_hi", 0, 0, tiled=True)
    projected = jnp.sum(received.astype(jnp.float32), axis=0)
    return projected.astype(jnp.bfloat16)[None]


def solution(mesh):
    shape = dict(mesh.shape)
    trio = 3
    split = jax.sharding.Mesh(
        mesh.devices.reshape(shape["span"], shape["seq"], shape["mp"] // trio, trio),
        ("span", "seq", "mp_hi", "mp_lo"),
    )
    mp = ("mp_hi", "mp_lo")
    in_specs = (
        P("span", "seq", mp),
        P("span", "seq", None),
        P("span", "seq", None),
        P("seq"),
        P(),
        P(mp, None),
    )
    out_specs = P("span", "seq", mp)
    return jax.shard_map(
        on_device, mesh=split, in_specs=in_specs, out_specs=out_specs, check_vma=False
    )
```

```python
import jax
import jax.numpy as jnp
from jax import lax
from jax.sharding import PartitionSpec as P

HEAD_DIM = 128
WINDOW = 3
GROUP = 6
KV_SLOTS = 2
CLIP_PAD = 16


def passed_along(x, axis, by):
    size = lax.axis_size(axis)
    pairs = [(i, i + by) for i in range(size) if 0 <= i + by < size]
    return lax.ppermute(x, axis, pairs)


def on_device(queries, keys, values, clip_ids, block_mask, out_weight):
    row_count = queries.shape[1]
    local_width = queries.shape[2]
    head_count = local_width // HEAD_DIM
    kv_count = keys.shape[2] // HEAD_DIM
    score_scale = HEAD_DIM ** (-0.5)
    span_index = lax.axis_index("span")
    first_head = lax.axis_index("mp") * head_count
    first_kv = jnp.minimum(first_head // GROUP, kv_count - KV_SLOTS)
    kv_slot = (first_head + jnp.arange(head_count, dtype=jnp.int32)) // GROUP - first_kv
    kv_start = first_kv * HEAD_DIM
    slot_width = KV_SLOTS * HEAD_DIM
    own_keys = lax.dynamic_slice_in_dim(keys[0], kv_start, slot_width, 1)
    own_values = lax.dynamic_slice_in_dim(values[0], kv_start, slot_width, 1)
    packed = jnp.concatenate([own_keys, own_values], axis=1)
    mask_row = lax.dynamic_index_in_dim(block_mask, span_index, 0, keepdims=False)
    visible = []
    for j in range(WINDOW):
        earlier = span_index - j
        entry = lax.dynamic_index_in_dim(mask_row, jnp.maximum(earlier, 0), 0, keepdims=False)
        visible.append(jnp.where(earlier >= 0, entry, 0))
    stacked = [packed]
    for j in range(1, WINDOW):
        stacked.append(passed_along(packed, "span", j))
    clip_row = jnp.zeros((CLIP_PAD, packed.shape[1]), jnp.bfloat16)
    clip_row = clip_row.at[0, :row_count].set(clip_ids.astype(jnp.bfloat16))
    outgoing = jnp.concatenate(stacked + [clip_row], axis=0)
    seq_count = lax.axis_size("seq")
    held = [outgoing]
    for shift in range(2, seq_count, 2):
        pairs = [(i, (i + shift) % seq_count) for i in range(seq_count)]
        held.append(lax.ppermute(outgoing, "seq", pairs))
    held = jnp.stack(held, axis=0)
    partner = lax.ppermute(held, "seq", [(i, i ^ 1) for i in range(seq_count)])
    query_heads = queries[0].reshape(row_count, head_count, HEAD_DIM)
    pick = kv_slot[:, None, None] == 0
    span_ok = jnp.stack(visible) == 1
    query_clips = clip_ids.astype(jnp.bfloat16)

    def piece_scores(piece):
        blocks = piece.shape[0]
        kv_rows = piece[:, : WINDOW * row_count].reshape(blocks, WINDOW, row_count, -1)
        key_clips = piece[:, WINDOW * row_count, :row_count].reshape(-1)
        rows = WINDOW * blocks * row_count
        kv = jnp.transpose(kv_rows, (1, 0, 2, 3)).reshape(rows, 2, KV_SLOTS, HEAD_DIM)
        s_both = jnp.einsum(
            "qhd,kad->ahqk", query_heads, kv[:, 0], preferred_element_type=jnp.float32
        )
        s = jnp.where(pick, s_both[0], s_both[1]) * score_scale
        same = query_clips[:, None, None] == key_clips[None, None, :]
        allowed = (span_ok[None, :, None] & same).reshape(row_count, rows)
        return jnp.where(allowed[None], s, -jnp.inf), kv[:, 1]

    def weighted(p, value_all):
        acc_both = jnp.einsum(
            "hqk,kad->ahqd", p.astype(jnp.bfloat16), value_all, preferred_element_type=jnp.float32
        )
        return jnp.where(pick, acc_both[0], acc_both[1])

    s, value_all = piece_scores(held)
    first_top = jnp.max(s, axis=2, keepdims=True)
    p = jnp.exp(s - first_top)
    first_total = jnp.sum(p, axis=2, keepdims=True)
    first_acc = weighted(p, value_all)
    partner, first_top, first_total, first_acc = lax.optimization_barrier(
        (partner, first_top, first_total, first_acc)
    )
    s, value_all = piece_scores(partner)
    top = jnp.maximum(first_top, jnp.max(s, axis=2, keepdims=True))
    p = jnp.exp(s - top)
    factor = jnp.exp(first_top - top)
    total = first_total * factor + jnp.sum(p, axis=2, keepdims=True)
    acc = first_acc * factor + weighted(p, value_all)
    attended = acc / total
    attended = (
        jnp.transpose(attended, (1, 0, 2)).reshape(row_count, local_width).astype(jnp.bfloat16)
    )
    mp_count = lax.axis_size("mp")
    out_width = out_weight.shape[1] // mp_count
    partial_sum = jnp.dot(attended, out_weight, preferred_element_type=jnp.float32)
    partial_sum = jnp.transpose(
        partial_sum.astype(jnp.bfloat16).reshape(row_count, mp_count, out_width), (1, 0, 2)
    )
    received = lax.all_to_all(partial_sum, "mp", 0, 0, tiled=True)
    projected = jnp.sum(received.astype(jnp.float32), axis=0)
    return projected.astype(jnp.bfloat16)[None]


def solution(mesh):
    in_specs = (
        P("span", "seq", "mp"),
        P("span", "seq", None),
        P("span", "seq", None),
        P("seq"),
        P(),
        P("mp", None),
    )
    out_specs = P("span", "seq", "mp")
    return jax.shard_map(
        on_device, mesh=mesh, in_specs=in_specs, out_specs=out_specs, check_vma=False
    )
```

```python
import jax
import jax.numpy as jnp
from jax import lax
from jax.sharding import PartitionSpec as P

HEAD_DIM = 128
WINDOW = 3
GROUP = 6
KV_SLOTS = 2
CLIP_PAD = 16


def passed_along(x, axis, by):
    size = lax.axis_size(axis)
    pairs = [(i, i + by) for i in range(size) if 0 <= i + by < size]
    return lax.ppermute(x, axis, pairs)


def on_device(queries, keys, values, clip_ids, block_mask, out_weight):
    row_count = queries.shape[1]
    local_width = queries.shape[2]
    head_count = local_width // HEAD_DIM
    kv_count = keys.shape[2] // HEAD_DIM
    score_scale = HEAD_DIM ** (-0.5)
    span_index = lax.axis_index("span")
    first_head = lax.axis_index("mp") * head_count
    first_kv = jnp.minimum(first_head // GROUP, kv_count - KV_SLOTS)
    kv_slot = (first_head + jnp.arange(head_count, dtype=jnp.int32)) // GROUP - first_kv
    kv_start = first_kv * HEAD_DIM
    slot_width = KV_SLOTS * HEAD_DIM
    own_keys = lax.dynamic_slice_in_dim(keys[0], kv_start, slot_width, 1)
    own_values = lax.dynamic_slice_in_dim(values[0], kv_start, slot_width, 1)
    packed = jnp.concatenate([own_keys, own_values], axis=1)
    mask_row = lax.dynamic_index_in_dim(block_mask, span_index, 0, keepdims=False)
    visible = []
    for j in range(WINDOW):
        earlier = span_index - j
        entry = lax.dynamic_index_in_dim(mask_row, jnp.maximum(earlier, 0), 0, keepdims=False)
        visible.append(jnp.where(earlier >= 0, entry, 0))
    stacked = [packed]
    for j in range(1, WINDOW):
        stacked.append(passed_along(packed, "span", j))
    clip_row = jnp.zeros((CLIP_PAD, packed.shape[1]), jnp.bfloat16)
    clip_row = clip_row.at[0, :row_count].set(clip_ids.astype(jnp.bfloat16))
    outgoing = jnp.concatenate(stacked + [clip_row], axis=0)
    seq_count = lax.axis_size("seq")
    held = [outgoing]
    for shift in range(2, seq_count, 2):
        pairs = [(i, (i + shift) % seq_count) for i in range(seq_count)]
        held.append(lax.ppermute(outgoing, "seq", pairs))
    held = jnp.stack(held, axis=0)
    partner = lax.ppermute(held, "seq", [(i, i ^ 1) for i in range(seq_count)])
    query_heads = queries[0].reshape(row_count, head_count, HEAD_DIM)
    pick = kv_slot[:, None, None] == 0
    span_ok = jnp.stack(visible) == 1
    query_clips = clip_ids.astype(jnp.bfloat16)

    def piece_scores(piece):
        blocks = piece.shape[0]
        kv_rows = piece[:, : WINDOW * row_count].reshape(blocks, WINDOW, row_count, -1)
        key_clips = piece[:, WINDOW * row_count, :row_count].reshape(-1)
        rows = WINDOW * blocks * row_count
        kv = jnp.transpose(kv_rows, (1, 0, 2, 3)).reshape(rows, 2, KV_SLOTS, HEAD_DIM)
        s_both = jnp.einsum(
            "qhd,kad->ahqk", query_heads, kv[:, 0], preferred_element_type=jnp.float32
        )
        s = jnp.where(pick, s_both[0], s_both[1]) * score_scale
        same = query_clips[:, None, None] == key_clips[None, None, :]
        allowed = (span_ok[None, :, None] & same).reshape(row_count, rows)
        return jnp.where(allowed[None], s, -jnp.inf), kv[:, 1]

    def weighted(p, value_all):
        acc_both = jnp.einsum(
            "hqk,kad->ahqd", p.astype(jnp.bfloat16), value_all, preferred_element_type=jnp.float32
        )
        return jnp.where(pick, acc_both[0], acc_both[1])

    s, value_all = piece_scores(held)
    first_top = jnp.max(s, axis=2, keepdims=True)
    p = jnp.exp(s - first_top)
    first_total = jnp.sum(p, axis=2, keepdims=True)
    first_acc = weighted(p, value_all)
    s, value_all = piece_scores(partner)
    top = jnp.maximum(first_top, jnp.max(s, axis=2, keepdims=True))
    p = jnp.exp(s - top)
    factor = jnp.exp(first_top - top)
    total = first_total * factor + jnp.sum(p, axis=2, keepdims=True)
    acc = first_acc * factor + weighted(p, value_all)
    attended = acc / total
    attended = (
        jnp.transpose(attended, (1, 0, 2)).reshape(row_count, local_width).astype(jnp.bfloat16)
    )
    mp_count = lax.axis_size("mp")
    out_width = out_weight.shape[1] // mp_count
    weight_parts = out_weight.reshape(local_width, mp_count, out_width)
    partial_sum = jnp.einsum(
        "qi,icj->qcj", attended, weight_parts, preferred_element_type=jnp.float32
    ).astype(jnp.bfloat16)
    received = lax.all_to_all(partial_sum, "mp", 1, 1, tiled=True)
    projected = jnp.sum(received.astype(jnp.float32), axis=1)
    return projected.astype(jnp.bfloat16)[None]


def solution(mesh):
    in_specs = (
        P("span", "seq", "mp"),
        P("span", "seq", None),
        P("span", "seq", None),
        P("seq"),
        P(),
        P("mp", None),
    )
    out_specs = P("span", "seq", "mp")
    return jax.shard_map(
        on_device, mesh=mesh, in_specs=in_specs, out_specs=out_specs, check_vma=False
    )
```

```python
import jax
import jax.numpy as jnp
from jax import lax
from jax.sharding import PartitionSpec as P

HEAD_DIM = 128
WINDOW = 3
GROUP = 6
KV_SLOTS = 2
CLIP_PAD = 16


def passed_along(x, axis, by):
    size = lax.axis_size(axis)
    pairs = [(i, i + by) for i in range(size) if 0 <= i + by < size]
    return lax.ppermute(x, axis, pairs)


def on_device(queries, keys, values, clip_ids, block_mask, out_weight):
    row_count = queries.shape[1]
    local_width = queries.shape[2]
    head_count = local_width // HEAD_DIM
    kv_count = keys.shape[2] // HEAD_DIM
    score_scale = HEAD_DIM ** (-0.5)
    span_index = lax.axis_index("span")
    first_head = lax.axis_index("mp") * head_count
    first_kv = jnp.minimum(first_head // GROUP, kv_count - KV_SLOTS)
    kv_slot = (first_head + jnp.arange(head_count, dtype=jnp.int32)) // GROUP - first_kv
    kv_start = first_kv * HEAD_DIM
    slot_width = KV_SLOTS * HEAD_DIM
    own_keys = lax.dynamic_slice_in_dim(keys[0], kv_start, slot_width, 1)
    own_values = lax.dynamic_slice_in_dim(values[0], kv_start, slot_width, 1)
    packed = jnp.concatenate([own_keys, own_values], axis=1)
    mask_row = lax.dynamic_index_in_dim(block_mask, span_index, 0, keepdims=False)
    visible = []
    for j in range(WINDOW):
        earlier = span_index - j
        entry = lax.dynamic_index_in_dim(mask_row, jnp.maximum(earlier, 0), 0, keepdims=False)
        visible.append(jnp.where(earlier >= 0, entry, 0))
    clip_row = jnp.zeros((CLIP_PAD, packed.shape[1]), jnp.bfloat16)
    clip_row = clip_row.at[0, :row_count].set(clip_ids.astype(jnp.bfloat16))
    own_block = jnp.concatenate([packed, clip_row], axis=0)
    shifted = jnp.concatenate([passed_along(packed, "span", j) for j in range(1, WINDOW)], axis=0)
    seq_count = lax.axis_size("seq")
    def same_core(block):
        held = [block]
        for shift in range(2, seq_count, 2):
            pairs = [(i, (i + shift) % seq_count) for i in range(seq_count)]
            held.append(lax.ppermute(block, "seq", pairs))
        return jnp.stack(held, axis=0)

    held = jnp.concatenate([same_core(own_block), same_core(shifted)], axis=1)
    partner = lax.ppermute(held, "seq", [(i, i ^ 1) for i in range(seq_count)])
    query_heads = queries[0].reshape(row_count, head_count, HEAD_DIM)
    pick = kv_slot[:, None, None] == 0
    span_ok = jnp.stack(visible) == 1
    query_clips = clip_ids.astype(jnp.bfloat16)

    def piece_scores(piece):
        blocks = piece.shape[0]
        own_rows = piece[:, None, :row_count]
        later_rows = piece[:, row_count + CLIP_PAD :].reshape(blocks, WINDOW - 1, row_count, -1)
        kv_rows = jnp.concatenate([own_rows, later_rows], axis=1)
        key_clips = piece[:, row_count, :row_count].reshape(-1)
        rows = WINDOW * blocks * row_count
        kv = jnp.transpose(kv_rows, (1, 0, 2, 3)).reshape(rows, 2, KV_SLOTS, HEAD_DIM)
        s_both = jnp.einsum(
            "qhd,kad->ahqk", query_heads, kv[:, 0], preferred_element_type=jnp.float32
        )
        s = jnp.where(pick, s_both[0], s_both[1]) * score_scale
        same = query_clips[:, None, None] == key_clips[None, None, :]
        allowed = (span_ok[None, :, None] & same).reshape(row_count, rows)
        return jnp.where(allowed[None], s, -jnp.inf), kv[:, 1]

    def weighted(p, value_all):
        acc_both = jnp.einsum(
            "hqk,kad->ahqd", p.astype(jnp.bfloat16), value_all, preferred_element_type=jnp.float32
        )
        return jnp.where(pick, acc_both[0], acc_both[1])

    s, value_all = piece_scores(held)
    first_top = jnp.max(s, axis=2, keepdims=True)
    p = jnp.exp(s - first_top)
    first_total = jnp.sum(p, axis=2, keepdims=True)
    first_acc = weighted(p, value_all)
    s, value_all = piece_scores(partner)
    top = jnp.maximum(first_top, jnp.max(s, axis=2, keepdims=True))
    p = jnp.exp(s - top)
    factor = jnp.exp(first_top - top)
    total = first_total * factor + jnp.sum(p, axis=2, keepdims=True)
    acc = first_acc * factor + weighted(p, value_all)
    attended = acc / total
    attended = (
        jnp.transpose(attended, (1, 0, 2)).reshape(row_count, local_width).astype(jnp.bfloat16)
    )
    mp_count = lax.axis_size("mp")
    out_width = out_weight.shape[1] // mp_count
    partial_sum = jnp.dot(attended, out_weight, preferred_element_type=jnp.float32)
    partial_sum = jnp.transpose(
        partial_sum.astype(jnp.bfloat16).reshape(row_count, mp_count, out_width), (1, 0, 2)
    )
    received = lax.all_to_all(partial_sum, "mp", 0, 0, tiled=True)
    projected = jnp.sum(received.astype(jnp.float32), axis=0)
    return projected.astype(jnp.bfloat16)[None]


def solution(mesh):
    in_specs = (
        P("span", "seq", "mp"),
        P("span", "seq", None),
        P("span", "seq", None),
        P("seq"),
        P(),
        P("mp", None),
    )
    out_specs = P("span", "seq", "mp")
    return jax.shard_map(
        on_device, mesh=mesh, in_specs=in_specs, out_specs=out_specs, check_vma=False
    )
```

```python
import jax
import jax.numpy as jnp
from jax import lax
from jax.sharding import PartitionSpec as P

HEAD_DIM = 128
WINDOW = 3
GROUP = 6
KV_SLOTS = 2
CLIP_PAD = 16


def passed_along(x, axis, by):
    size = lax.axis_size(axis)
    pairs = [(i, i + by) for i in range(size) if 0 <= i + by < size]
    return lax.ppermute(x, axis, pairs)


def on_device(queries, keys, values, clip_ids, block_mask, out_weight):
    row_count = queries.shape[1]
    local_width = queries.shape[2]
    head_count = local_width // HEAD_DIM
    kv_count = keys.shape[2] // HEAD_DIM
    score_scale = HEAD_DIM ** (-0.5)
    span_index = lax.axis_index("span")
    first_head = lax.axis_index("mp") * head_count
    first_kv = jnp.minimum(first_head // GROUP, kv_count - KV_SLOTS)
    kv_slot = (first_head + jnp.arange(head_count, dtype=jnp.int32)) // GROUP - first_kv
    kv_start = first_kv * HEAD_DIM
    slot_width = KV_SLOTS * HEAD_DIM
    own_keys = lax.dynamic_slice_in_dim(keys[0], kv_start, slot_width, 1)
    own_values = lax.dynamic_slice_in_dim(values[0], kv_start, slot_width, 1)
    packed = jnp.concatenate([own_keys, own_values], axis=1)
    mask_row = lax.dynamic_index_in_dim(block_mask, span_index, 0, keepdims=False)
    visible = []
    for j in range(WINDOW):
        earlier = span_index - j
        entry = lax.dynamic_index_in_dim(mask_row, jnp.maximum(earlier, 0), 0, keepdims=False)
        visible.append(jnp.where(earlier >= 0, entry, 0))
    stacked = [packed]
    for j in range(1, WINDOW):
        stacked.append(passed_along(packed, "span", j))
    clip_row = jnp.zeros((CLIP_PAD, packed.shape[1]), jnp.bfloat16)
    clip_row = clip_row.at[0, :row_count].set(clip_ids.astype(jnp.bfloat16))
    outgoing = jnp.concatenate(stacked + [clip_row], axis=0)
    seq_count = lax.axis_size("seq")
    fetched = []
    for shift in range(2, seq_count, 2):
        pairs = [(i, (i + shift) % seq_count) for i in range(seq_count)]
        fetched.append(lax.ppermute(outgoing, "seq", pairs))
    pieces = [outgoing[None]] + ([jnp.stack(fetched, axis=0)] if fetched else [])
    held = jnp.concatenate(pieces, axis=0)
    partner = lax.ppermute(held, "seq", [(i, i ^ 1) for i in range(seq_count)])
    query_heads = queries[0].reshape(row_count, head_count, HEAD_DIM)
    pick = kv_slot[:, None, None] == 0
    span_ok = jnp.stack(visible) == 1
    query_clips = clip_ids.astype(jnp.bfloat16)

    def piece_scores(piece):
        blocks = piece.shape[0]
        kv_rows = piece[:, : WINDOW * row_count].reshape(blocks, WINDOW, row_count, -1)
        key_clips = piece[:, WINDOW * row_count, :row_count].reshape(-1)
        rows = WINDOW * blocks * row_count
        kv = jnp.transpose(kv_rows, (1, 0, 2, 3)).reshape(rows, 2, KV_SLOTS, HEAD_DIM)
        s_both = jnp.einsum(
            "qhd,kad->ahqk", query_heads, kv[:, 0], preferred_element_type=jnp.float32
        )
        s = jnp.where(pick, s_both[0], s_both[1]) * score_scale
        same = query_clips[:, None, None] == key_clips[None, None, :]
        allowed = (span_ok[None, :, None] & same).reshape(row_count, rows)
        return jnp.where(allowed[None], s, -jnp.inf), kv[:, 1]

    def weighted(p, value_all):
        acc_both = jnp.einsum(
            "hqk,kad->ahqd", p.astype(jnp.bfloat16), value_all, preferred_element_type=jnp.float32
        )
        return jnp.where(pick, acc_both[0], acc_both[1])

    top = total = acc = None
    for piece in pieces + [partner]:
        s, value_all = piece_scores(piece)
        piece_top = jnp.max(s, axis=2, keepdims=True)
        if top is None:
            top = piece_top
            p = jnp.exp(s - top)
            total = jnp.sum(p, axis=2, keepdims=True)
            acc = weighted(p, value_all)
            continue
        new_top = jnp.maximum(top, piece_top)
        p = jnp.exp(s - new_top)
        factor = jnp.exp(top - new_top)
        total = total * factor + jnp.sum(p, axis=2, keepdims=True)
        acc = acc * factor + weighted(p, value_all)
        top = new_top
    attended = acc / total
    attended = (
        jnp.transpose(attended, (1, 0, 2)).reshape(row_count, local_width).astype(jnp.bfloat16)
    )
    mp_count = lax.axis_size("mp")
    out_width = out_weight.shape[1] // mp_count
    partial_sum = jnp.dot(attended, out_weight, preferred_element_type=jnp.float32)
    partial_sum = jnp.transpose(
        partial_sum.astype(jnp.bfloat16).reshape(row_count, mp_count, out_width), (1, 0, 2)
    )
    received = lax.all_to_all(partial_sum, "mp", 0, 0, tiled=True)
    projected = jnp.sum(received.astype(jnp.float32), axis=0)
    return projected.astype(jnp.bfloat16)[None]


def solution(mesh):
    in_specs = (
        P("span", "seq", "mp"),
        P("span", "seq", None),
        P("span", "seq", None),
        P("seq"),
        P(),
        P("mp", None),
    )
    out_specs = P("span", "seq", "mp")
    return jax.shard_map(
        on_device, mesh=mesh, in_specs=in_specs, out_specs=out_specs, check_vma=False
    )
```
